256 devices in a mesh: coil: 4 (over x_hi, core), slab: 64 (over z, y, x_lo).
Axes of the slice: x: 4 (x_hi: 2, x_lo: 2; x = x_hi * 2 + x_lo), y: 4, z: 8, core: 2. Of those that a mesh axis runs over, the one named last changes fastest.
Arguments:
- partial_time: bfloat16 [4, 4, 128, 512, 1024], P('coil', None, 'slab'), may hold values from -6 to 6
- brain_mask: int32 [512], P(('coil', 'slab')), may hold values from 0 to 1, as said below
- rank_limit: int32 [512], P(('coil', 'slab')), may hold values from 2 to 16
- start_basis: float32 [16, 1024], replicated, may hold values from -6 to 6
Outputs:
- denoised: bfloat16 [512, 512, 1024], P(('coil', 'slab'))
The draws below stay inside these ranges and needn't reach their ends.
Inputs may be any that keep to these rules, and one draw needn't show every extreme that they name: `brain_mask`: A patch p can be 1 only if its slab position (p // 2) mod 64 lies in the middle half, from 16 up to 47.
All inputs are finite; a program needn't handle non-finite values.
Results may differ from the reference program's by a relative error of at most 0.023.
Values may be sent and summed in bfloat16 or wider, within the bound.
No kernel may reach another device: no remote copies, remote signals or barrier semaphores. Data moves between devices by JAX's collectives and lax.ppermute only.
A program may use at most 128 MiB of HBM per device.

```python
import math
import jax
import jax.numpy as jnp
from jax import lax

SPEC = 512
PVOX = 512
RANK_MAX = 16
ITERS = 4
PATCH_DEV = 2
NP = 512
N_COIL = 4
N_SLAB = 64


def draw_brain_mask(key, part):
    patch_index = jnp.arange(PATCH_DEV * N_COIL * N_SLAB, dtype=jnp.int32)
    slab_index = patch_index // PATCH_DEV % N_SLAB
    inside = (slab_index >= N_SLAB // 4) & (slab_index < N_SLAB - N_SLAB // 4)
    chance = jax.random.randint(key, patch_index.shape, 0, 10)
    return jnp.where(inside & (chance < 9), 1, 0).astype(jnp.int32)


def plant(entries, own_key, low, high):
    place = [jax.random.randint(jax.random.fold_in(own_key, axis), (), 0, length) for axis, length in enumerate(entries.shape)]
    widest = entries.shape.index(max(entries.shape))
    next_to = place[:widest] + [(place[widest] + 1) % entries.shape[widest]] + place[widest + 1:]
    return entries.at[tuple(place)].set(low).at[tuple(next_to)].set(high)


def block_levels(rng, dims, pieces, least, top_value):
    def one(dim, blocks):
        heights = jax.random.uniform(jax.random.fold_in(jax.random.fold_in(rng, 6), dim), (blocks,), jnp.float32, least / len(pieces), top_value / len(pieces))
        return jnp.repeat(jnp.exp(heights), dims[dim] // blocks).reshape((-1,) + (1,) * (len(dims) - dim - 1))

    loudness = one(*pieces[0])
    for cut in pieces[1:]:
        loudness = loudness * one(*cut)
    return loudness


def gaussian(key, extent, deviation, limit, shards=(), held_as=jnp.bfloat16):
    array = deviation * jax.random.normal(key, extent, jnp.float32)
    if shards:
        array = array * block_levels(key, extent, shards, -0.22, 0.18)
    return jnp.clip(array, -limit, limit).astype(held_as)


def setup_inputs(seed: int = 0) -> dict:
    key_of = jax.random.split(jax.random.key(seed), 5)
    partial_time = gaussian(key_of[0], (N_COIL, N_COIL, N_SLAB * PATCH_DEV, PVOX, 2 * SPEC), 1.0, 6.0, ((0, 4), (2, 64)))
    brain_mask = draw_brain_mask(jax.random.fold_in(key_of[4], 71), 0)
    rank_limit = plant(jax.random.randint(key_of[2], (NP,), 2, RANK_MAX + 1), jax.random.fold_in(key_of[2], 1), 2, RANK_MAX).astype(jnp.int32)
    start_basis = gaussian(key_of[3], (RANK_MAX, 2 * SPEC), 1.0, 6.0, (), jnp.float32)
    return {"partial_time": partial_time, "brain_mask": brain_mask, "rank_limit": rank_limit, "start_basis": start_basis}


def spectral_table(length):
    points = jnp.arange(length, dtype=jnp.int32)
    phase_index = points[:, None] * points[None, :] % length
    angles = phase_index.astype(jnp.float32) * (2.0 * math.pi / length)
    cosine = jnp.cos(angles) / math.sqrt(length)
    sine_part = jnp.sin(angles) / math.sqrt(length)
    upper_rows = jnp.concatenate([cosine, -sine_part], axis=1)
    lower_rows = jnp.concatenate([sine_part, cosine], axis=1)
    return jnp.concatenate([upper_rows, lower_rows], axis=0).astype(jnp.bfloat16)

def denoise_patch(patch_block, rank_cap, transform, start_basis):
    spectra = jnp.dot(patch_block.astype(jnp.float32), transform.astype(jnp.float32), preferred_element_type=jnp.float32)
    spectral_gram = lax.dot_general(spectra, spectra, (((0,), (0,)), ((), ())), precision=lax.Precision.HIGHEST)
    subspace = start_basis
    for sweep_index in range(ITERS):
        product_rows = jnp.dot(subspace, spectral_gram, precision=lax.Precision.HIGHEST)
        inner_gram = jnp.dot(product_rows, product_rows.T, precision=lax.Precision.HIGHEST)
        factor = jnp.linalg.cholesky(inner_gram)
        subspace = jax.scipy.linalg.solve_triangular(factor, product_rows, lower=True)
    keep_rows = jnp.arange(subspace.shape[0], dtype=jnp.int32) < rank_cap
    truncated = jnp.where(keep_rows[:, None], subspace, jnp.zeros_like(subspace))
    coefficients = lax.dot_general(truncated, spectra, (((1,), (1,)), ((), ())), precision=lax.Precision.HIGHEST)
    result = lax.dot_general(coefficients, truncated, (((0,), (0,)), ((), ())), precision=lax.Precision.HIGHEST)
    return result.astype(jnp.bfloat16)

def reference(partial_time, brain_mask, rank_limit, start_basis):
    summed = lax.optimization_barrier(jnp.sum(partial_time.astype(jnp.float32), axis=0)).astype(jnp.bfloat16)
    patches = summed.reshape((-1, PVOX, 2 * SPEC))
    transform = spectral_table(SPEC)

    def denoise_item(packed):
        patch_block, active, rank_cap = packed
        return lax.cond(active > 0, lambda: denoise_patch(patch_block, rank_cap, transform, start_basis), lambda: jnp.zeros(patch_block.shape, jnp.bfloat16))
    return lax.map(denoise_item, (patches, brain_mask, rank_limit))
```

```python
import math

import jax
import jax.numpy as jnp
from jax import lax
from jax.sharding import PartitionSpec as P

ITERS = 4
HI = lax.Precision.HIGHEST


def spectral_table(length):
    points = jnp.arange(length, dtype=jnp.int32)
    phase_index = points[:, None] * points[None, :] % length
    angles = phase_index.astype(jnp.float32) * (2.0 * math.pi / length)
    cosine = jnp.cos(angles) / math.sqrt(length)
    sine_part = jnp.sin(angles) / math.sqrt(length)
    upper_rows = jnp.concatenate([cosine, -sine_part], axis=1)
    lower_rows = jnp.concatenate([sine_part, cosine], axis=1)
    return jnp.concatenate([upper_rows, lower_rows], axis=0).astype(jnp.bfloat16)


def denoise_batch(patches, flags, ranks, transform, start_basis):
    spectra = jnp.einsum("bvt,tf->bvf", patches, transform, preferred_element_type=jnp.float32)
    kernel = jnp.einsum("bvf,bwf->bvw", spectra, spectra, precision=HI)
    coeff = jnp.einsum("kf,bvf->bkv", start_basis, spectra, precision=HI)
    for sweep_index in range(ITERS):
        pushed = jnp.einsum("bkv,bvw->bkw", coeff, kernel, precision=HI)
        inner_gram = jnp.einsum("bkw,bjw->bkj", pushed, coeff, precision=HI)
        factor = jnp.linalg.cholesky(inner_gram)
        if sweep_index < ITERS - 1:
            coeff = jax.scipy.linalg.solve_triangular(factor, pushed, lower=True)
        else:
            image = jnp.einsum("bkv,bvf->bkf", coeff, spectra, precision=HI)
            both = jax.scipy.linalg.solve_triangular(
                factor, jnp.concatenate([pushed, image], axis=-1), lower=True
            )
            coeff = both[..., : pushed.shape[-1]]
            subspace = both[..., pushed.shape[-1]:]
    keep_rows = jnp.arange(subspace.shape[1], dtype=jnp.int32)[None, :, None] < ranks[:, None, None]
    truncated = jnp.where(keep_rows, subspace, 0.0)
    coefficients = jnp.where(keep_rows, coeff, 0.0)
    result = jnp.einsum("bkv,bkf->bvf", coefficients, truncated, precision=HI)
    result = result.astype(jnp.bfloat16)
    return jnp.where(flags[:, None, None], result, jnp.zeros_like(result))


def body(partial_time, brain_mask, rank_limit, start_basis):
    summed = lax.psum_scatter(partial_time, "coil", scatter_dimension=1, tiled=True)
    patches = summed.reshape((-1, summed.shape[-2], summed.shape[-1]))
    transform = spectral_table(patches.shape[-1] // 2)
    return denoise_batch(patches, brain_mask > 0, rank_limit, transform, start_basis)


def solution(mesh):
    return jax.shard_map(
        body,
        mesh=mesh,
        in_specs=(
            P("coil", None, "slab", None, None),
            P(("coil", "slab")),
            P(("coil", "slab")),
            P(),
        ),
        out_specs=P(("coil", "slab"), None, None),
        check_vma=False,
    )
```

```python
import math

import jax
import jax.numpy as jnp
from jax import lax
from jax.sharding import PartitionSpec as P

ITERS = 4
HI = lax.Precision.HIGHEST


def spectral_table(length):
    points = jnp.arange(length, dtype=jnp.int32)
    phase_index = points[:, None] * points[None, :] % length
    angles = phase_index.astype(jnp.float32) * (2.0 * math.pi / length)
    cosine = jnp.cos(angles) / math.sqrt(length)
    sine_part = jnp.sin(angles) / math.sqrt(length)
    upper_rows = jnp.concatenate([cosine, -sine_part], axis=1)
    lower_rows = jnp.concatenate([sine_part, cosine], axis=1)
    return jnp.concatenate([upper_rows, lower_rows], axis=0).astype(jnp.bfloat16)


def denoise_batch(patches, flags, ranks, transform, start_basis):
    spectra = jnp.einsum("bvt,tf->bvf", patches, transform, preferred_element_type=jnp.float32)
    kernel = jnp.einsum("bvf,bwf->bvw", spectra, spectra, precision=HI)
    coeff = jnp.einsum("kf,bvf->bkv", start_basis, spectra, precision=HI)
    for sweep_index in range(ITERS):
        pushed = jnp.einsum("bkv,bvw->bkw", coeff, kernel, precision=HI)
        inner_gram = jnp.einsum("bkw,bjw->bkj", pushed, coeff, precision=HI)
        factor = jnp.linalg.cholesky(inner_gram)
        if sweep_index < ITERS - 1:
            coeff = jax.scipy.linalg.solve_triangular(factor, pushed, lower=True)
        else:
            image = jnp.einsum("bkv,bvf->bkf", coeff, spectra, precision=HI)
            both = jax.scipy.linalg.solve_triangular(
                factor, jnp.concatenate([pushed, image], axis=-1), lower=True
            )
            coeff = both[..., : pushed.shape[-1]]
            subspace = both[..., pushed.shape[-1]:]
    keep_rows = jnp.arange(subspace.shape[1], dtype=jnp.int32)[None, :, None] < ranks[:, None, None]
    truncated = jnp.where(keep_rows, subspace, 0.0)
    coefficients = jnp.where(keep_rows, coeff, 0.0)
    result = jnp.einsum("bkv,bkf->bvf", coefficients, truncated, precision=HI)
    result = result.astype(jnp.bfloat16)
    return jnp.where(flags[:, None, None], result, jnp.zeros_like(result))


def ring_pairs(n_coil, n_slab):
    pairs = []
    for coil in range(n_coil):
        x_hi, core = divmod(coil, 2)
        for slab in range(n_slab):
            x_lo = slab % 2
            x = 2 * x_hi + x_lo
            step = 1 if core == 0 else -1
            x_to = (x + step) % 4
            coil_to = 2 * (x_to // 2) + core
            slab_to = slab - x_lo + x_to % 2
            pairs.append((coil * n_slab + slab, coil_to * n_slab + slab_to))
    return pairs


def coil_sum(partial_time, n_coil, n_slab):
    parts = partial_time[0]
    coil = lax.axis_index("coil")
    chip_pair = [(i, i ^ 1) for i in range(n_coil)]

    def pick(o):
        return lax.dynamic_index_in_dim(parts, o, 0, keepdims=False)

    got_forward = lax.ppermute(pick(coil ^ 3), "coil", chip_pair)
    forward = (pick(coil ^ 2).astype(jnp.float32) + got_forward.astype(jnp.float32)).astype(jnp.bfloat16)
    got_own = lax.ppermute(pick(coil ^ 1), "coil", chip_pair)
    own = pick(coil).astype(jnp.float32) + got_own.astype(jnp.float32)
    pairs = ring_pairs(n_coil, n_slab)
    hop = lax.ppermute(forward, ("coil", "slab"), pairs)
    hop = lax.ppermute(hop, ("coil", "slab"), pairs)
    return (own + hop.astype(jnp.float32)).astype(jnp.bfloat16)


def make_body(n_coil, n_slab):
    def body(partial_time, brain_mask, rank_limit, start_basis):
        patches = coil_sum(partial_time, n_coil, n_slab)
        transform = spectral_table(patches.shape[-1] // 2)
        return denoise_batch(patches, brain_mask > 0, rank_limit, transform, start_basis)

    return body


def solution(mesh):
    return jax.shard_map(
        make_body(mesh.shape["coil"], mesh.shape["slab"]),
        mesh=mesh,
        in_specs=(
            P("coil", None, "slab", None, None),
            P(("coil", "slab")),
            P(("coil", "slab")),
            P(),
        ),
        out_specs=P(("coil", "slab"), None, None),
        check_vma=False,
    )
```

```python
import math

import jax
import jax.numpy as jnp
from jax import lax
from jax.experimental import pallas as pl
from jax.sharding import PartitionSpec as P

ITERS = 4
HI = lax.Precision.HIGHEST


def spectral_table(length):
    points = jnp.arange(length, dtype=jnp.int32)
    phase_index = points[:, None] * points[None, :] % length
    angles = phase_index.astype(jnp.float32) * (2.0 * math.pi / length)
    cosine = jnp.cos(angles) / math.sqrt(length)
    sine_part = jnp.sin(angles) / math.sqrt(length)
    upper_rows = jnp.concatenate([cosine, -sine_part], axis=1)
    lower_rows = jnp.concatenate([sine_part, cosine], axis=1)
    return jnp.concatenate([upper_rows, lower_rows], axis=0).astype(jnp.bfloat16)


def factor_solve_kernel(gram_ref, rhs_ref, out_ref):
    for item in range(gram_ref.shape[0]):
        gram = gram_ref[item]
        work = rhs_ref[item]
        for col in range(gram.shape[0]):
            scale = 1.0 / jnp.sqrt(gram[col:col + 1, col:col + 1])
            column = gram[:, col:col + 1] * scale
            row = gram[col:col + 1, :] * scale
            solved = work[col:col + 1, :] * scale
            out_ref[item, col:col + 1, :] = solved
            gram = gram - column * row
            work = work - column * solved


def factor_solve(inner_gram, rhs):
    sym = 0.5 * (inner_gram + jnp.swapaxes(inner_gram, -1, -2))
    return pl.pallas_call(
        factor_solve_kernel,
        out_shape=jax.ShapeDtypeStruct(rhs.shape, jnp.float32),
    )(sym, rhs)


def denoise_batch(patches, flags, ranks, transform, start_basis):
    spectra = jnp.einsum("bvt,tf->bvf", patches, transform, preferred_element_type=jnp.float32)
    kernel = jnp.einsum("bvf,bwf->bvw", spectra, spectra, precision=HI)
    coeff = jnp.einsum("kf,bvf->bkv", start_basis, spectra, precision=HI)
    for sweep_index in range(ITERS):
        pushed = jnp.einsum("bkv,bvw->bkw", coeff, kernel, precision=HI)
        inner_gram = jnp.einsum("bkw,bjw->bkj", pushed, coeff, precision=HI)
        if sweep_index < ITERS - 1:
            coeff = factor_solve(inner_gram, pushed)
        else:
            image = jnp.einsum("bkv,bvf->bkf", coeff, spectra, precision=HI)
            both = factor_solve(inner_gram, jnp.concatenate([pushed, image], axis=-1))
            coeff = both[..., : pushed.shape[-1]]
            subspace = both[..., pushed.shape[-1]:]
    keep_rows = jnp.arange(subspace.shape[1], dtype=jnp.int32)[None, :, None] < ranks[:, None, None]
    truncated = jnp.where(keep_rows, subspace, 0.0)
    coefficients = jnp.where(keep_rows, coeff, 0.0)
    result = jnp.einsum("bkv,bkf->bvf", coefficients, truncated, precision=HI)
    result = result.astype(jnp.bfloat16)
    return jnp.where(flags[:, None, None], result, jnp.zeros_like(result))


def ring_pairs(n_coil, n_slab):
    pairs = []
    for coil in range(n_coil):
        x_hi, core = divmod(coil, 2)
        for slab in range(n_slab):
            x_lo = slab % 2
            x = 2 * x_hi + x_lo
            step = 1 if core == 0 else -1
            x_to = (x + step) % 4
            coil_to = 2 * (x_to // 2) + core
            slab_to = slab - x_lo + x_to % 2
            pairs.append((coil * n_slab + slab, coil_to * n_slab + slab_to))
    return pairs


def coil_sum(partial_time, n_coil, n_slab):
    parts = partial_time[0]
    coil = lax.axis_index("coil")
    chip_pair = [(i, i ^ 1) for i in range(n_coil)]

    def pick(o):
        return lax.dynamic_index_in_dim(parts, o, 0, keepdims=False)

    got_forward = lax.ppermute(pick(coil ^ 3), "coil", chip_pair)
    forward = (pick(coil ^ 2).astype(jnp.float32) + got_forward.astype(jnp.float32)).astype(jnp.bfloat16)
    got_own = lax.ppermute(pick(coil ^ 1), "coil", chip_pair)
    own = pick(coil).astype(jnp.float32) + got_own.astype(jnp.float32)
    pairs = ring_pairs(n_coil, n_slab)
    hop = lax.ppermute(forward, ("coil", "slab"), pairs)
    hop = lax.ppermute(hop, ("coil", "slab"), pairs)
    return (own + hop.astype(jnp.float32)).astype(jnp.bfloat16)


def make_body(n_coil, n_slab):
    def body(partial_time, brain_mask, rank_limit, start_basis):
        patches = coil_sum(partial_time, n_coil, n_slab)
        transform = spectral_table(patches.shape[-1] // 2)
        return denoise_batch(patches, brain_mask > 0, rank_limit, transform, start_basis)

    return body


def solution(mesh):
    return jax.shard_map(
        make_body(mesh.shape["coil"], mesh.shape["slab"]),
        mesh=mesh,
        in_specs=(
            P("coil", None, "slab", None, None),
            P(("coil", "slab")),
            P(("coil", "slab")),
            P(),
        ),
        out_specs=P(("coil", "slab"), None, None),
        check_vma=False,
    )
```

```python
import math

import jax
import jax.numpy as jnp
from jax import lax
from jax.experimental import pallas as pl
from jax.sharding import PartitionSpec as P

ITERS = 4
HI = lax.Precision.HIGH


def spectral_table(length):
    points = jnp.arange(length, dtype=jnp.int32)
    phase_index = points[:, None] * points[None, :] % length
    angles = phase_index.astype(jnp.float32) * (2.0 * math.pi / length)
    cosine = jnp.cos(angles) / math.sqrt(length)
    sine_part = jnp.sin(angles) / math.sqrt(length)
    upper_rows = jnp.concatenate([cosine, -sine_part], axis=1)
    lower_rows = jnp.concatenate([sine_part, cosine], axis=1)
    return jnp.concatenate([upper_rows, lower_rows], axis=0).astype(jnp.bfloat16)


def factor_solve_kernel(gram_ref, rhs_ref, out_ref):
    items = range(gram_ref.shape[0])
    grams = [gram_ref[item] for item in items]
    works = [rhs_ref[item] for item in items]
    for col in range(grams[0].shape[0]):
        for item in items:
            gram, work = grams[item], works[item]
            scale = 1.0 / jnp.sqrt(gram[col:col + 1, col:col + 1])
            column = gram[:, col:col + 1] * scale
            row = gram[col:col + 1, :] * scale
            solved = work[col:col + 1, :] * scale
            out_ref[item, col:col + 1, :] = solved
            grams[item] = gram - column * row
            works[item] = work - column * solved


def factor_solve(inner_gram, rhs):
    sym = 0.5 * (inner_gram + jnp.swapaxes(inner_gram, -1, -2))
    return pl.pallas_call(
        factor_solve_kernel,
        out_shape=jax.ShapeDtypeStruct(rhs.shape, jnp.float32),
    )(sym, rhs)


def denoise_batch(patches, flags, ranks, transform, start_basis):
    spectra = jnp.einsum("bvt,tf->bvf", patches, transform, preferred_element_type=jnp.float32)
    kernel = jnp.einsum("bvf,bwf->bvw", spectra, spectra, precision=HI)
    coeff = jnp.einsum("kf,bvf->bkv", start_basis, spectra, precision=HI)
    for sweep_index in range(ITERS):
        pushed = jnp.einsum("bkv,bvw->bkw", coeff, kernel, precision=HI)
        inner_gram = jnp.einsum("bkw,bjw->bkj", pushed, coeff, precision=HI)
        if sweep_index < ITERS - 1:
            coeff = factor_solve(inner_gram, pushed)
        else:
            image = jnp.einsum("bkv,bvf->bkf", coeff, spectra, precision=HI)
            both = factor_solve(inner_gram, jnp.concatenate([pushed, image], axis=-1))
            coeff = both[..., : pushed.shape[-1]]
            subspace = both[..., pushed.shape[-1]:]
    keep_rows = jnp.arange(subspace.shape[1], dtype=jnp.int32)[None, :, None] < ranks[:, None, None]
    truncated = jnp.where(keep_rows, subspace, 0.0)
    coefficients = jnp.where(keep_rows, coeff, 0.0)
    result = jnp.einsum("bkv,bkf->bvf", coefficients, truncated, precision=HI)
    result = result.astype(jnp.bfloat16)
    return jnp.where(flags[:, None, None], result, jnp.zeros_like(result))


def ring_pairs(n_coil, n_slab):
    pairs = []
    for coil in range(n_coil):
        x_hi, core = divmod(coil, 2)
        for slab in range(n_slab):
            x_lo = slab % 2
            x = 2 * x_hi + x_lo
            step = 1 if core == 0 else -1
            x_to = (x + step) % 4
            coil_to = 2 * (x_to // 2) + core
            slab_to = slab - x_lo + x_to % 2
            pairs.append((coil * n_slab + slab, coil_to * n_slab + slab_to))
    return pairs


def coil_sum(partial_time, n_coil, n_slab):
    parts = partial_time[0]
    coil = lax.axis_index("coil")
    chip_pair = [(i, i ^ 1) for i in range(n_coil)]

    def pick(o):
        return lax.dynamic_index_in_dim(parts, o, 0, keepdims=False)

    got_forward = lax.ppermute(pick(coil ^ 3), "coil", chip_pair)
    forward = (pick(coil ^ 2).astype(jnp.float32) + got_forward.astype(jnp.float32)).astype(jnp.bfloat16)
    got_own = lax.ppermute(pick(coil ^ 1), "coil", chip_pair)
    own = pick(coil).astype(jnp.float32) + got_own.astype(jnp.float32)
    pairs = ring_pairs(n_coil, n_slab)
    hop = lax.ppermute(forward, ("coil", "slab"), pairs)
    hop = lax.ppermute(hop, ("coil", "slab"), pairs)
    return (own + hop.astype(jnp.float32)).astype(jnp.bfloat16)


def make_body(n_coil, n_slab):
    def body(partial_time, brain_mask, rank_limit, start_basis):
        patches = coil_sum(partial_time, n_coil, n_slab)
        transform = spectral_table(patches.shape[-1] // 2)
        return denoise_batch(patches, brain_mask > 0, rank_limit, transform, start_basis)

    return body


def solution(mesh):
    return jax.shard_map(
        make_body(mesh.shape["coil"], mesh.shape["slab"]),
        mesh=mesh,
        in_specs=(
            P("coil", None, "slab", None, None),
            P(("coil", "slab")),
            P(("coil", "slab")),
            P(),
        ),
        out_specs=P(("coil", "slab"), None, None),
        check_vma=False,
    )
```

```python
import math

import jax
import jax.numpy as jnp
from jax import lax
from jax.experimental import pallas as pl
from jax.sharding import PartitionSpec as P

ITERS = 4
HI = lax.Precision.HIGH


def spectral_table(length):
    points = jnp.arange(length, dtype=jnp.int32)
    phase_index = points[:, None] * points[None, :] % length
    angles = phase_index.astype(jnp.float32) * (2.0 * math.pi / length)
    cosine = jnp.cos(angles) / math.sqrt(length)
    sine_part = jnp.sin(angles) / math.sqrt(length)
    upper_rows = jnp.concatenate([cosine, -sine_part], axis=1)
    lower_rows = jnp.concatenate([sine_part, cosine], axis=1)
    return jnp.concatenate([upper_rows, lower_rows], axis=0).astype(jnp.bfloat16)


def factor_solve_kernel(gram_ref, rhs_ref, out_ref):
    items = range(gram_ref.shape[0])
    grams = [gram_ref[item] for item in items]
    works = [rhs_ref[item] for item in items]
    for col in range(grams[0].shape[0]):
        for item in items:
            gram, work = grams[item], works[item]
            scale = 1.0 / jnp.sqrt(gram[col:col + 1, col:col + 1])
            column = gram[:, col:col + 1] * scale
            row = gram[col:col + 1, :] * scale
            solved = work[col:col + 1, :] * scale
            out_ref[item, col:col + 1, :] = solved
            grams[item] = gram - column * row
            works[item] = work - column * solved


def factor_solve(inner_gram, rhs):
    sym = 0.5 * (inner_gram + jnp.swapaxes(inner_gram, -1, -2))
    return pl.pallas_call(
        factor_solve_kernel,
        out_shape=jax.ShapeDtypeStruct(rhs.shape, jnp.float32),
    )(sym, rhs)


def denoise_batch(patches, flags, ranks, transform, start_basis):
    spectra = jnp.einsum("bvt,tf->bvf", patches, transform, preferred_element_type=jnp.float32)
    kernel = jnp.einsum("bvf,bwf->bvw", spectra, spectra, precision=HI)
    coeff = jnp.einsum("kf,bvf->bkv", start_basis, spectra, precision=HI)
    for sweep_index in range(ITERS):
        pushed = jnp.einsum("bkv,bvw->bkw", coeff, kernel, precision=HI)
        inner_gram = jnp.einsum("bkw,bjw->bkj", pushed, coeff, precision=HI)
        if sweep_index < ITERS - 1:
            coeff = factor_solve(inner_gram, pushed)
        else:
            image = jnp.einsum("bkv,bvf->bkf", coeff, spectra, precision=HI)
            both = factor_solve(inner_gram, jnp.concatenate([pushed, image], axis=-1))
            coeff = both[..., : pushed.shape[-1]]
            subspace = both[..., pushed.shape[-1]:]
    keep_rows = jnp.arange(subspace.shape[1], dtype=jnp.int32)[None, :, None] < ranks[:, None, None]
    truncated = jnp.where(keep_rows, subspace, 0.0)
    coefficients = jnp.where(keep_rows, coeff, 0.0)
    result = jnp.einsum("bkv,bkf->bvf", coefficients, truncated, precision=HI)
    result = result.astype(jnp.bfloat16)
    return jnp.where(flags[:, None, None], result, jnp.zeros_like(result))


def ring_pairs(n_coil, n_slab):
    pairs = []
    for coil in range(n_coil):
        x_hi, core = divmod(coil, 2)
        for slab in range(n_slab):
            x_lo = slab % 2
            x = 2 * x_hi + x_lo
            step = 1 if core == 0 else -1
            x_to = (x + step) % 4
            coil_to = 2 * (x_to // 2) + core
            slab_to = slab - x_lo + x_to % 2
            pairs.append((coil * n_slab + slab, coil_to * n_slab + slab_to))
    return pairs


def coil_sum(partial_time, n_coil, n_slab):
    coil = lax.axis_index("coil")
    chip_pair = [(i, i ^ 1) for i in range(n_coil)]
    pairs = ring_pairs(n_coil, n_slab)
    sums = []
    arrived = None
    for q in range(partial_time.shape[2]):
        parts = partial_time[0, :, q]

        def pick(o):
            return lax.dynamic_index_in_dim(parts, o, 0, keepdims=False)

        got_forward = lax.ppermute(pick(coil ^ 3), "coil", chip_pair)
        forward = (pick(coil ^ 2).astype(jnp.float32) + got_forward.astype(jnp.float32)).astype(jnp.bfloat16)
        got_own = lax.ppermute(pick(coil ^ 1), "coil", chip_pair)
        own = pick(coil).astype(jnp.float32) + got_own.astype(jnp.float32)
        if arrived is not None:
            forward, arrived = lax.optimization_barrier((forward, arrived))
            sums[-1] = (sums[-1][0], arrived)
        hop = lax.ppermute(forward, ("coil", "slab"), pairs)
        hop = lax.ppermute(hop, ("coil", "slab"), pairs)
        arrived = hop
        sums.append((own, hop))
    return sums


def make_body(n_coil, n_slab):
    def body(partial_time, brain_mask, rank_limit, start_basis):
        transform = spectral_table(partial_time.shape[-1] // 2)
        flags = brain_mask > 0
        pieces = coil_sum(partial_time, n_coil, n_slab)
        outs = []
        for q, (own, hop) in enumerate(pieces):
            patch = (own + hop.astype(jnp.float32)).astype(jnp.bfloat16)
            outs.append(denoise_batch(patch[None], flags[q:q + 1], rank_limit[q:q + 1], transform, start_basis))
        return jnp.concatenate(outs, axis=0)

    return body


def solution(mesh):
    return jax.shard_map(
        make_body(mesh.shape["coil"], mesh.shape["slab"]),
        mesh=mesh,
        in_specs=(
            P("coil", None, "slab", None, None),
            P(("coil", "slab")),
            P(("coil", "slab")),
            P(),
        ),
        out_specs=P(("coil", "slab"), None, None),
        check_vma=False,
    )
```

```python
import math

import jax
import jax.numpy as jnp
from jax import lax
from jax.experimental import pallas as pl
from jax.sharding import PartitionSpec as P

ITERS = 4
HI = lax.Precision.HIGH


def spectral_table(length):
    points = jnp.arange(length, dtype=jnp.int32)
    phase_index = points[:, None] * points[None, :] % length
    angles = phase_index.astype(jnp.float32) * (2.0 * math.pi / length)
    cosine = jnp.cos(angles) / math.sqrt(length)
    sine_part = jnp.sin(angles) / math.sqrt(length)
    upper_rows = jnp.concatenate([cosine, -sine_part], axis=1)
    lower_rows = jnp.concatenate([sine_part, cosine], axis=1)
    return jnp.concatenate([upper_rows, lower_rows], axis=0).astype(jnp.bfloat16)


def factor_solve_kernel(gram_ref, rhs_ref, out_ref):
    items = range(gram_ref.shape[0])
    grams = [gram_ref[item] for item in items]
    works = [rhs_ref[item] for item in items]
    for col in range(grams[0].shape[0]):
        for item in items:
            gram, work = grams[item], works[item]
            scale = 1.0 / jnp.sqrt(gram[col:col + 1, col:col + 1])
            column = gram[:, col:col + 1] * scale
            row = gram[col:col + 1, :] * scale
            solved = work[col:col + 1, :] * scale
            out_ref[item, col:col + 1, :] = solved
            grams[item] = gram - column * row
            works[item] = work - column * solved


def factor_solve(inner_gram, rhs):
    sym = 0.5 * (inner_gram + jnp.swapaxes(inner_gram, -1, -2))
    return pl.pallas_call(
        factor_solve_kernel,
        out_shape=jax.ShapeDtypeStruct(rhs.shape, jnp.float32),
    )(sym, rhs)


def denoise_batch(patches, flags, ranks, transform, start_basis):
    spectra = jnp.einsum("bvt,tf->bvf", patches, transform, preferred_element_type=jnp.float32)
    kernel = jnp.einsum("bvf,bwf->bvw", spectra, spectra, precision=HI)
    coeff = jnp.einsum("kf,bvf->bkv", start_basis, spectra, precision=HI)
    for sweep_index in range(ITERS):
        pushed = jnp.einsum("bkv,bvw->bkw", coeff, kernel, precision=HI)
        inner_gram = jnp.einsum("bkw,bjw->bkj", pushed, coeff, precision=HI)
        if sweep_index < ITERS - 1:
            coeff = factor_solve(inner_gram, pushed)
        else:
            image = jnp.einsum("bkv,bvf->bkf", coeff, spectra, precision=HI)
            both = factor_solve(inner_gram, jnp.concatenate([pushed, image], axis=-1))
            coeff = both[..., : pushed.shape[-1]]
            subspace = both[..., pushed.shape[-1]:]
    keep_rows = jnp.arange(subspace.shape[1], dtype=jnp.int32)[None, :, None] < ranks[:, None, None]
    truncated = jnp.where(keep_rows, subspace, 0.0)
    coefficients = jnp.where(keep_rows, coeff, 0.0)
    result = jnp.einsum("bkv,bkf->bvf", coefficients, truncated, precision=HI)
    result = result.astype(jnp.bfloat16)
    return jnp.where(flags[:, None, None], result, jnp.zeros_like(result))


def ring_pairs(n_coil, n_slab):
    pairs = []
    for coil in range(n_coil):
        x_hi, core = divmod(coil, 2)
        for slab in range(n_slab):
            x_lo = slab % 2
            x = 2 * x_hi + x_lo
            step = 1 if core == 0 else -1
            x_to = (x + step) % 4
            coil_to = 2 * (x_to // 2) + core
            slab_to = slab - x_lo + x_to % 2
            pairs.append((coil * n_slab + slab, coil_to * n_slab + slab_to))
    return pairs


def coil_sum(partial_time, n_coil, n_slab):
    coil = lax.axis_index("coil")
    chip_pair = [(i, i ^ 1) for i in range(n_coil)]
    pairs = ring_pairs(n_coil, n_slab)
    sums = []
    for q in range(partial_time.shape[2]):
        parts = partial_time[0, :, q]

        def pick(o):
            return lax.dynamic_index_in_dim(parts, o, 0, keepdims=False)

        got_forward = lax.ppermute(pick(coil ^ 3), "coil", chip_pair)
        forward = (pick(coil ^ 2).astype(jnp.float32) + got_forward.astype(jnp.float32)).astype(jnp.bfloat16)
        got_own = lax.ppermute(pick(coil ^ 1), "coil", chip_pair)
        own = pick(coil).astype(jnp.float32) + got_own.astype(jnp.float32)
        hop = lax.ppermute(forward, ("coil", "slab"), pairs)
        hop = lax.ppermute(hop, ("coil", "slab"), pairs)
        sums.append((own, hop))
    return sums


def make_body(n_coil, n_slab):
    def body(partial_time, brain_mask, rank_limit, start_basis):
        transform = spectral_table(partial_time.shape[-1] // 2)
        flags = brain_mask > 0
        pieces = coil_sum(partial_time, n_coil, n_slab)
        patches = jnp.stack([(own + hop.astype(jnp.float32)).astype(jnp.bfloat16) for own, hop in pieces])
        return denoise_batch(patches, flags, rank_limit, transform, start_basis)

    return body


def solution(mesh):
    return jax.shard_map(
        make_body(mesh.shape["coil"], mesh.shape["slab"]),
        mesh=mesh,
        in_specs=(
            P("coil", None, "slab", None, None),
            P(("coil", "slab")),
            P(("coil", "slab")),
            P(),
        ),
        out_specs=P(("coil", "slab"), None, None),
        check_vma=False,
    )
```

```python
import math

import jax
import jax.numpy as jnp
from jax import lax
from jax.experimental import pallas as pl
from jax.sharding import PartitionSpec as P

ITERS = 4
HI = lax.Precision.HIGH


def spectral_table(length):
    points = jnp.arange(length, dtype=jnp.int32)
    phase_index = points[:, None] * points[None, :] % length
    angles = phase_index.astype(jnp.float32) * (2.0 * math.pi / length)
    cosine = jnp.cos(angles) / math.sqrt(length)
    sine_part = jnp.sin(angles) / math.sqrt(length)
    upper_rows = jnp.concatenate([cosine, -sine_part], axis=1)
    lower_rows = jnp.concatenate([sine_part, cosine], axis=1)
    return jnp.concatenate([upper_rows, lower_rows], axis=0).astype(jnp.bfloat16)


def factor_solve_kernel(gram_ref, rhs_ref, out_ref):
    items = range(gram_ref.shape[0])
    grams = [gram_ref[item] for item in items]
    works = [rhs_ref[item] for item in items]
    for col in range(grams[0].shape[0]):
        for item in items:
            gram, work = grams[item], works[item]
            scale = 1.0 / jnp.sqrt(gram[col:col + 1, col:col + 1])
            column = gram[:, col:col + 1] * scale
            row = gram[col:col + 1, :] * scale
            solved = work[col:col + 1, :] * scale
            out_ref[item, col:col + 1, :] = solved
            grams[item] = gram - column * row
            works[item] = work - column * solved


def factor_solve(inner_gram, rhs):
    sym = 0.5 * (inner_gram + jnp.swapaxes(inner_gram, -1, -2))
    return pl.pallas_call(
        factor_solve_kernel,
        out_shape=jax.ShapeDtypeStruct(rhs.shape, jnp.float32),
    )(sym, rhs)


def denoise_batch(patches, flags, ranks, transform, start_basis):
    spectra = jnp.einsum("bvt,tf->bvf", patches, transform, preferred_element_type=jnp.float32)
    kernel = jnp.einsum("bvf,bwf->bvw", spectra, spectra, precision=HI)
    coeff = jnp.einsum("kf,bvf->bkv", start_basis, spectra, precision=HI)
    for sweep_index in range(ITERS):
        pushed = jnp.einsum("bkv,bvw->bkw", coeff, kernel, precision=HI)
        inner_gram = jnp.einsum("bkw,bjw->bkj", pushed, coeff, precision=HI)
        if sweep_index < ITERS - 1:
            coeff = factor_solve(inner_gram, pushed)
        else:
            image = jnp.einsum("bkv,bvf->bkf", coeff, spectra, precision=HI)
            both = factor_solve(inner_gram, jnp.concatenate([pushed, image], axis=-1))
            coeff = both[..., : pushed.shape[-1]]
            subspace = both[..., pushed.shape[-1]:]
    keep_rows = jnp.arange(subspace.shape[1], dtype=jnp.int32)[None, :, None] < ranks[:, None, None]
    truncated = jnp.where(keep_rows, subspace, 0.0)
    coefficients = jnp.where(keep_rows, coeff, 0.0)
    result = jnp.einsum("bkv,bkf->bvf", coefficients, truncated, precision=HI)
    result = result.astype(jnp.bfloat16)
    return jnp.where(flags[:, None, None], result, jnp.zeros_like(result))


def ring_pairs(n_coil, n_slab):
    pairs = []
    for coil in range(n_coil):
        x_hi, core = divmod(coil, 2)
        for slab in range(n_slab):
            x_lo = slab % 2
            x = 2 * x_hi + x_lo
            step = 1 if core == 0 else -1
            x_to = (x + step) % 4
            coil_to = 2 * (x_to // 2) + core
            slab_to = slab - x_lo + x_to % 2
            pairs.append((coil * n_slab + slab, coil_to * n_slab + slab_to))
    return pairs


def coil_sum(partial_time, n_coil, n_slab):
    coil = lax.axis_index("coil")
    chip_pair = [(i, i ^ 1) for i in range(n_coil)]
    pairs = ring_pairs(n_coil, n_slab)
    sums = []
    for q in range(partial_time.shape[2]):

        def pick(o, q=q):
            block = lax.dynamic_slice(partial_time, (0, o, q, 0, 0), (1, 1, 1) + partial_time.shape[3:])
            return block.reshape(partial_time.shape[3:])

        got_forward = lax.ppermute(pick(coil ^ 3), "coil", chip_pair)
        forward = (pick(coil ^ 2).astype(jnp.float32) + got_forward.astype(jnp.float32)).astype(jnp.bfloat16)
        got_own = lax.ppermute(pick(coil ^ 1), "coil", chip_pair)
        own = pick(coil).astype(jnp.float32) + got_own.astype(jnp.float32)
        hop = lax.ppermute(forward, ("coil", "slab"), pairs)
        hop = lax.ppermute(hop, ("coil", "slab"), pairs)
        sums.append((own, hop))
    return sums


def make_body(n_coil, n_slab):
    def body(partial_time, brain_mask, rank_limit, start_basis):
        transform = spectral_table(partial_time.shape[-1] // 2)
        flags = brain_mask > 0
        pieces = coil_sum(partial_time, n_coil, n_slab)
        patches = jnp.stack([(own + hop.astype(jnp.float32)).astype(jnp.bfloat16) for own, hop in pieces])
        return denoise_batch(patches, flags, rank_limit, transform, start_basis)

    return body


def solution(mesh):
    return jax.shard_map(
        make_body(mesh.shape["coil"], mesh.shape["slab"]),
        mesh=mesh,
        in_specs=(
            P("coil", None, "slab", None, None),
            P(("coil", "slab")),
            P(("coil", "slab")),
            P(),
        ),
        out_specs=P(("coil", "slab"), None, None),
        check_vma=False,
    )
```

```python
import math

import jax
import jax.numpy as jnp
from jax import lax
from jax.experimental import pallas as pl
from jax.sharding import PartitionSpec as P

ITERS = 4
HI = lax.Precision.HIGH


def spectral_table(length):
    points = jnp.arange(length, dtype=jnp.int32)
    phase_index = points[:, None] * points[None, :] % length
    angles = phase_index.astype(jnp.float32) * (2.0 * math.pi / length)
    cosine = jnp.cos(angles) / math.sqrt(length)
    sine_part = jnp.sin(angles) / math.sqrt(length)
    upper_rows = jnp.concatenate([cosine, -sine_part], axis=1)
    lower_rows = jnp.concatenate([sine_part, cosine], axis=1)
    return jnp.concatenate([upper_rows, lower_rows], axis=0).astype(jnp.bfloat16)


def factor_solve_kernel(gram_ref, rhs_ref, out_ref):
    items = range(gram_ref.shape[0])
    grams = [gram_ref[item] for item in items]
    works = [rhs_ref[item] for item in items]
    for col in range(grams[0].shape[0]):
        for item in items:
            gram, work = grams[item], works[item]
            scale = 1.0 / jnp.sqrt(gram[col:col + 1, col:col + 1])
            column = gram[:, col:col + 1] * scale
            row = gram[col:col + 1, :] * scale
            solved = work[col:col + 1, :] * scale
            out_ref[item, col:col + 1, :] = solved
            grams[item] = gram - column * row
            works[item] = work - column * solved


def factor_solve(inner_gram, rhs):
    sym = 0.5 * (inner_gram + jnp.swapaxes(inner_gram, -1, -2))
    return pl.pallas_call(
        factor_solve_kernel,
        out_shape=jax.ShapeDtypeStruct(rhs.shape, jnp.float32),
    )(sym, rhs)


def denoise_batch(patches, flags, ranks, transform, start_basis):
    spectra = jnp.einsum("bvt,tf->bvf", patches, transform, preferred_element_type=jnp.float32)
    kernel = jnp.einsum("bvf,bwf->bvw", spectra, spectra, precision=HI)
    coeff = jnp.einsum("kf,bvf->bkv", start_basis, spectra, precision=HI)
    for sweep_index in range(ITERS):
        pushed = jnp.einsum("bkv,bvw->bkw", coeff, kernel, precision=HI)
        inner_gram = jnp.einsum("bkw,bjw->bkj", pushed, coeff, precision=HI)
        if sweep_index < ITERS - 1:
            coeff = factor_solve(inner_gram, pushed)
        else:
            image = jnp.einsum("bkv,bvf->bkf", coeff, spectra, precision=HI)
            both = factor_solve(inner_gram, jnp.concatenate([pushed, image], axis=-1))
            coeff = both[..., : pushed.shape[-1]]
            subspace = both[..., pushed.shape[-1]:]
    keep_rows = jnp.arange(subspace.shape[1], dtype=jnp.int32)[None, :, None] < ranks[:, None, None]
    truncated = jnp.where(keep_rows, subspace, 0.0)
    coefficients = jnp.where(keep_rows, coeff, 0.0)
    result = jnp.einsum("bkv,bkf->bvf", coefficients, truncated, precision=HI)
    result = result.astype(jnp.bfloat16)
    return jnp.where(flags[:, None, None], result, jnp.zeros_like(result))


def ring_pairs(n_coil, n_slab):
    pairs = []
    for coil in range(n_coil):
        x_hi, core = divmod(coil, 2)
        for slab in range(n_slab):
            x_lo = slab % 2
            x = 2 * x_hi + x_lo
            step = 1 if core == 0 else -1
            x_to = (x + step) % 4
            coil_to = 2 * (x_to // 2) + core
            slab_to = slab - x_lo + x_to % 2
            pairs.append((coil * n_slab + slab, coil_to * n_slab + slab_to))
    return pairs


def coil_sum(partial_time, n_coil, n_slab):
    coil = lax.axis_index("coil")
    chip_pair = [(i, i ^ 1) for i in range(n_coil)]
    pairs = ring_pairs(n_coil, n_slab)
    sums = []
    source = [partial_time]
    for q in range(partial_time.shape[2]):

        def pick(o, q=q):
            block = lax.dynamic_slice(source[0], (0, o, q, 0, 0), (1, 1, 1) + source[0].shape[3:])
            return block.reshape(source[0].shape[3:])

        got_forward = lax.ppermute(pick(coil ^ 3), "coil", chip_pair)
        forward = (pick(coil ^ 2).astype(jnp.float32) + got_forward.astype(jnp.float32)).astype(jnp.bfloat16)
        source[0], forward = lax.optimization_barrier((source[0], forward))
        got_own = lax.ppermute(pick(coil ^ 1), "coil", chip_pair)
        own = pick(coil).astype(jnp.float32) + got_own.astype(jnp.float32)
        hop = lax.ppermute(forward, ("coil", "slab"), pairs)
        hop = lax.ppermute(hop, ("coil", "slab"), pairs)
        sums.append((own, hop))
    return sums


def make_body(n_coil, n_slab):
    def body(partial_time, brain_mask, rank_limit, start_basis):
        transform = spectral_table(partial_time.shape[-1] // 2)
        flags = brain_mask > 0
        pieces = coil_sum(partial_time, n_coil, n_slab)
        patches = jnp.stack([(own + hop.astype(jnp.float32)).astype(jnp.bfloat16) for own, hop in pieces])
        return denoise_batch(patches, flags, rank_limit, transform, start_basis)

    return body


def solution(mesh):
    return jax.shard_map(
        make_body(mesh.shape["coil"], mesh.shape["slab"]),
        mesh=mesh,
        in_specs=(
            P("coil", None, "slab", None, None),
            P(("coil", "slab")),
            P(("coil", "slab")),
            P(),
        ),
        out_specs=P(("coil", "slab"), None, None),
        check_vma=False,
    )
```

```python
import math

import jax
import jax.numpy as jnp
from jax import lax
from jax.experimental import pallas as pl
from jax.sharding import PartitionSpec as P

ITERS = 4
HI = lax.Precision.HIGH


def spectral_table(length):
    points = jnp.arange(length, dtype=jnp.int32)
    phase_index = points[:, None] * points[None, :] % length
    angles = phase_index.astype(jnp.float32) * (2.0 * math.pi / length)
    cosine = jnp.cos(angles) / math.sqrt(length)
    sine_part = jnp.sin(angles) / math.sqrt(length)
    upper_rows = jnp.concatenate([cosine, -sine_part], axis=1)
    lower_rows = jnp.concatenate([sine_part, cosine], axis=1)
    return jnp.concatenate([upper_rows, lower_rows], axis=0).astype(jnp.bfloat16)


def factor_solve_kernel(gram_ref, rhs_ref, out_ref):
    items = range(gram_ref.shape[0])
    grams = [gram_ref[item] for item in items]
    works = [rhs_ref[item] for item in items]
    for col in range(grams[0].shape[0]):
        for item in items:
            gram, work = grams[item], works[item]
            scale = 1.0 / jnp.sqrt(gram[col:col + 1, col:col + 1])
            column = gram[:, col:col + 1] * scale
            row = gram[col:col + 1, :] * scale
            solved = work[col:col + 1, :] * scale
            out_ref[item, col:col + 1, :] = solved
            grams[item] = gram - column * row
            works[item] = work - column * solved


def factor_solve(inner_gram, rhs):
    sym = 0.5 * (inner_gram + jnp.swapaxes(inner_gram, -1, -2))
    return pl.pallas_call(
        factor_solve_kernel,
        out_shape=jax.ShapeDtypeStruct(rhs.shape, jnp.float32),
    )(sym, rhs)


def denoise_batch(patches, flags, ranks, transform, start_basis):
    spectra = jnp.einsum("bvt,tf->bvf", patches, transform, preferred_element_type=jnp.float32)
    kernel = jnp.einsum("bvf,bwf->bvw", spectra, spectra, precision=HI)
    coeff = jnp.einsum("kf,bvf->bkv", start_basis, spectra, precision=HI)
    for sweep_index in range(ITERS):
        pushed = jnp.einsum("bkv,bvw->bkw", coeff, kernel, precision=HI)
        inner_gram = jnp.einsum("bkw,bjw->bkj", pushed, coeff, precision=HI)
        if sweep_index < ITERS - 1:
            coeff = factor_solve(inner_gram, pushed)
        else:
            image = jnp.einsum("bkv,bvf->bkf", coeff, spectra, preferred_element_type=jnp.float32)
            both = factor_solve(inner_gram, jnp.concatenate([pushed, image], axis=-1))
            coeff = both[..., : pushed.shape[-1]]
            subspace = both[..., pushed.shape[-1]:]
    keep_rows = jnp.arange(subspace.shape[1], dtype=jnp.int32)[None, :, None] < ranks[:, None, None]
    truncated = jnp.where(keep_rows, subspace, 0.0)
    coefficients = jnp.where(keep_rows, coeff, 0.0)
    result = jnp.einsum("bkv,bkf->bvf", coefficients, truncated, preferred_element_type=jnp.float32)
    result = result.astype(jnp.bfloat16)
    return jnp.where(flags[:, None, None], result, jnp.zeros_like(result))


def ring_pairs(n_coil, n_slab):
    pairs = []
    for coil in range(n_coil):
        x_hi, core = divmod(coil, 2)
        for slab in range(n_slab):
            x_lo = slab % 2
            x = 2 * x_hi + x_lo
            step = 1 if core == 0 else -1
            x_to = (x + step) % 4
            coil_to = 2 * (x_to // 2) + core
            slab_to = slab - x_lo + x_to % 2
            pairs.append((coil * n_slab + slab, coil_to * n_slab + slab_to))
    return pairs


def coil_sum(partial_time, n_coil, n_slab):
    coil = lax.axis_index("coil")
    chip_pair = [(i, i ^ 1) for i in range(n_coil)]
    pairs = ring_pairs(n_coil, n_slab)
    sums = []
    for q in range(partial_time.shape[2]):

        def pick(o, q=q):
            block = lax.dynamic_slice(partial_time, (0, o, q, 0, 0), (1, 1, 1) + partial_time.shape[3:])
            return block.reshape(partial_time.shape[3:])

        got_forward = lax.ppermute(pick(coil ^ 3), "coil", chip_pair)
        forward = (pick(coil ^ 2).astype(jnp.float32) + got_forward.astype(jnp.float32)).astype(jnp.bfloat16)
        got_own = lax.ppermute(pick(coil ^ 1), "coil", chip_pair)
        own = pick(coil).astype(jnp.float32) + got_own.astype(jnp.float32)
        hop = lax.ppermute(forward, ("coil", "slab"), pairs)
        hop = lax.ppermute(hop, ("coil", "slab"), pairs)
        sums.append((own, hop))
    return sums


def make_body(n_coil, n_slab):
    def body(partial_time, brain_mask, rank_limit, start_basis):
        transform = spectral_table(partial_time.shape[-1] // 2)
        flags = brain_mask > 0
        pieces = coil_sum(partial_time, n_coil, n_slab)
        patches = jnp.stack([(own + hop.astype(jnp.float32)).astype(jnp.bfloat16) for own, hop in pieces])
        return denoise_batch(patches, flags, rank_limit, transform, start_basis)

    return body


def solution(mesh):
    return jax.shard_map(
        make_body(mesh.shape["coil"], mesh.shape["slab"]),
        mesh=mesh,
        in_specs=(
            P("coil", None, "slab", None, None),
            P(("coil", "slab")),
            P(("coil", "slab")),
            P(),
        ),
        out_specs=P(("coil", "slab"), None, None),
        check_vma=False,
    )
```

```python
import math

import jax
import jax.numpy as jnp
from jax import lax
from jax.experimental import pallas as pl
from jax.sharding import PartitionSpec as P

ITERS = 4
HI = lax.Precision.HIGH


def spectral_table(length):
    points = jnp.arange(length, dtype=jnp.int32)
    phase_index = points[:, None] * points[None, :] % length
    angles = phase_index.astype(jnp.float32) * (2.0 * math.pi / length)
    cosine = jnp.cos(angles) / math.sqrt(length)
    sine_part = jnp.sin(angles) / math.sqrt(length)
    upper_rows = jnp.concatenate([cosine, -sine_part], axis=1)
    lower_rows = jnp.concatenate([sine_part, cosine], axis=1)
    return jnp.concatenate([upper_rows, lower_rows], axis=0).astype(jnp.bfloat16)


def factor_solve_kernel(gram_ref, rhs_ref, out_ref):
    items = range(gram_ref.shape[0])
    grams = [gram_ref[item] for item in items]
    works = [rhs_ref[item] for item in items]
    for col in range(grams[0].shape[0]):
        for item in items:
            gram, work = grams[item], works[item]
            scale = 1.0 / jnp.sqrt(gram[col:col + 1, col:col + 1])
            column = gram[:, col:col + 1] * scale
            row = gram[col:col + 1, :] * scale
            solved = work[col:col + 1, :] * scale
            out_ref[item, col:col + 1, :] = solved
            grams[item] = gram - column * row
            works[item] = work - column * solved


def factor_solve(inner_gram, rhs):
    sym = 0.5 * (inner_gram + jnp.swapaxes(inner_gram, -1, -2))
    return pl.pallas_call(
        factor_solve_kernel,
        out_shape=jax.ShapeDtypeStruct(rhs.shape, jnp.float32),
    )(sym, rhs)


def denoise_batch(spectra, flags, ranks, start_basis):
    kernel = jnp.einsum("bvf,bwf->bvw", spectra, spectra, precision=HI)
    coeff = jnp.einsum("kf,bvf->bkv", start_basis, spectra, precision=HI)
    for sweep_index in range(ITERS):
        pushed = jnp.einsum("bkv,bvw->bkw", coeff, kernel, precision=HI)
        inner_gram = jnp.einsum("bkw,bjw->bkj", pushed, coeff, precision=HI)
        if sweep_index < ITERS - 1:
            coeff = factor_solve(inner_gram, pushed)
        else:
            image = jnp.einsum("bkv,bvf->bkf", coeff, spectra, preferred_element_type=jnp.float32)
            both = factor_solve(inner_gram, jnp.concatenate([pushed, image], axis=-1))
            coeff = both[..., : pushed.shape[-1]]
            subspace = both[..., pushed.shape[-1]:]
    keep_rows = jnp.arange(subspace.shape[1], dtype=jnp.int32)[None, :, None] < ranks[:, None, None]
    truncated = jnp.where(keep_rows, subspace, 0.0)
    coefficients = jnp.where(keep_rows, coeff, 0.0)
    result = jnp.einsum("bkv,bkf->bvf", coefficients, truncated, preferred_element_type=jnp.float32)
    result = result.astype(jnp.bfloat16)
    return jnp.where(flags[:, None, None], result, jnp.zeros_like(result))


def ring_pairs(n_coil, n_slab):
    pairs = []
    for coil in range(n_coil):
        x_hi, core = divmod(coil, 2)
        for slab in range(n_slab):
            x_lo = slab % 2
            x = 2 * x_hi + x_lo
            step = 1 if core == 0 else -1
            x_to = (x + step) % 4
            coil_to = 2 * (x_to // 2) + core
            slab_to = slab - x_lo + x_to % 2
            pairs.append((coil * n_slab + slab, coil_to * n_slab + slab_to))
    return pairs


def coil_sum(partial_time, n_coil, n_slab):
    coil = lax.axis_index("coil")
    chip_pair = [(i, i ^ 1) for i in range(n_coil)]
    pairs = ring_pairs(n_coil, n_slab)
    sums = []
    for q in range(partial_time.shape[2]):

        def pick(o, q=q):
            block = lax.dynamic_slice(partial_time, (0, o, q, 0, 0), (1, 1, 1) + partial_time.shape[3:])
            return block.reshape(partial_time.shape[3:])

        got_forward = lax.ppermute(pick(coil ^ 3), "coil", chip_pair)
        forward = (pick(coil ^ 2).astype(jnp.float32) + got_forward.astype(jnp.float32)).astype(jnp.bfloat16)
        got_own = lax.ppermute(pick(coil ^ 1), "coil", chip_pair)
        own = pick(coil).astype(jnp.float32) + got_own.astype(jnp.float32)
        hop = lax.ppermute(forward, ("coil", "slab"), pairs)
        hop = lax.ppermute(hop, ("coil", "slab"), pairs)
        sums.append((own, hop))
    return sums


def make_body(n_coil, n_slab):
    def body(partial_time, brain_mask, rank_limit, start_basis):
        transform = spectral_table(partial_time.shape[-1] // 2)
        flags = brain_mask > 0
        pieces = coil_sum(partial_time, n_coil, n_slab)
        owns = jnp.stack([own.astype(jnp.bfloat16) for own, hop in pieces])
        hops = jnp.stack([hop for own, hop in pieces])
        spectra = jnp.einsum("bvt,tf->bvf", owns, transform, preferred_element_type=jnp.float32)
        spectra = spectra + jnp.einsum("bvt,tf->bvf", hops, transform, preferred_element_type=jnp.float32)
        return denoise_batch(spectra, flags, rank_limit, start_basis)

    return body


def solution(mesh):
    return jax.shard_map(
        make_body(mesh.shape["coil"], mesh.shape["slab"]),
        mesh=mesh,
        in_specs=(
            P("coil", None, "slab", None, None),
            P(("coil", "slab")),
            P(("coil", "slab")),
            P(),
        ),
        out_specs=P(("coil", "slab"), None, None),
        check_vma=False,
    )
```

```python
import math

import jax
import jax.numpy as jnp
from jax import lax
from jax.experimental import pallas as pl
from jax.sharding import PartitionSpec as P

ITERS = 4
HI = lax.Precision.HIGH


def spectral_table(length):
    points = jnp.arange(length, dtype=jnp.int32)
    phase_index = points[:, None] * points[None, :] % length
    angles = phase_index.astype(jnp.float32) * (2.0 * math.pi / length)
    cosine = jnp.cos(angles) / math.sqrt(length)
    sine_part = jnp.sin(angles) / math.sqrt(length)
    upper_rows = jnp.concatenate([cosine, -sine_part], axis=1)
    lower_rows = jnp.concatenate([sine_part, cosine], axis=1)
    return jnp.concatenate([upper_rows, lower_rows], axis=0).astype(jnp.bfloat16)


def factor_solve_kernel(gram_ref, rhs_ref, out_ref):
    items = range(gram_ref.shape[0])
    grams = [gram_ref[item] for item in items]
    works = [rhs_ref[item] for item in items]
    for col in range(grams[0].shape[0]):
        for item in items:
            gram, work = grams[item], works[item]
            scale = 1.0 / jnp.sqrt(gram[col:col + 1, col:col + 1])
            column = gram[:, col:col + 1] * scale
            row = gram[col:col + 1, :] * scale
            solved = work[col:col + 1, :] * scale
            out_ref[item, col:col + 1, :] = solved
            grams[item] = gram - column * row
            works[item] = work - column * solved


def factor_solve(inner_gram, rhs):
    sym = 0.5 * (inner_gram + jnp.swapaxes(inner_gram, -1, -2))
    return pl.pallas_call(
        factor_solve_kernel,
        out_shape=jax.ShapeDtypeStruct(rhs.shape, jnp.float32),
    )(sym, rhs)


def denoise_batch(spectra, flags, ranks, start_basis):
    kernel = jnp.einsum("bvf,bwf->bvw", spectra, spectra, precision=HI)
    coeff = jnp.einsum("kf,bvf->bkv", start_basis, spectra, precision=HI)
    for sweep_index in range(ITERS):
        pushed = jnp.einsum("bkv,bvw->bkw", coeff, kernel, precision=HI)
        inner_gram = jnp.einsum("bkw,bjw->bkj", pushed, coeff, precision=HI)
        if sweep_index < ITERS - 1:
            coeff = factor_solve(inner_gram, pushed)
        else:
            image = jnp.einsum("bkv,bvf->bkf", coeff, spectra, preferred_element_type=jnp.float32)
            both = factor_solve(inner_gram, jnp.concatenate([pushed, image], axis=-1))
            coeff = both[..., : pushed.shape[-1]]
            subspace = both[..., pushed.shape[-1]:]
    keep_rows = jnp.arange(subspace.shape[1], dtype=jnp.int32)[None, :, None] < ranks[:, None, None]
    truncated = jnp.where(keep_rows, subspace, 0.0)
    coefficients = jnp.where(keep_rows, coeff, 0.0)
    result = jnp.einsum("bkv,bkf->bvf", coefficients, truncated, preferred_element_type=jnp.float32)
    result = result.astype(jnp.bfloat16)
    return jnp.where(flags[:, None, None], result, jnp.zeros_like(result))


def ring_pairs(n_coil, n_slab):
    pairs = []
    for coil in range(n_coil):
        x_hi, core = divmod(coil, 2)
        for slab in range(n_slab):
            x_lo = slab % 2
            x = 2 * x_hi + x_lo
            step = 1 if core == 0 else -1
            x_to = (x + step) % 4
            coil_to = 2 * (x_to // 2) + core
            slab_to = slab - x_lo + x_to % 2
            pairs.append((coil * n_slab + slab, coil_to * n_slab + slab_to))
    return pairs


def coil_sum(partial_time, n_coil, n_slab):
    coil = lax.axis_index("coil")
    chip_pair = [(i, i ^ 1) for i in range(n_coil)]
    pairs = ring_pairs(n_coil, n_slab)
    patch_count = partial_time.shape[2]

    def pick(source, o, q):
        block = lax.dynamic_slice(source, (0, o, q, 0, 0), (1, 1, 1) + source.shape[3:])
        return block.reshape(source.shape[3:])

    forwards = []
    for q in range(patch_count):
        got_forward = lax.ppermute(pick(partial_time, coil ^ 3, q), "coil", chip_pair)
        forward = pick(partial_time, coil ^ 2, q).astype(jnp.float32) + got_forward.astype(jnp.float32)
        forwards.append(forward.astype(jnp.bfloat16))
    source, forwards = lax.optimization_barrier((partial_time, forwards))
    sums = []
    for q in range(patch_count):
        hop = lax.ppermute(forwards[q], ("coil", "slab"), pairs)
        hop = lax.ppermute(hop, ("coil", "slab"), pairs)
        got_own = lax.ppermute(pick(source, coil ^ 1, q), "coil", chip_pair)
        own = pick(source, coil, q).astype(jnp.float32) + got_own.astype(jnp.float32)
        sums.append((own, hop))
    return sums


def make_body(n_coil, n_slab):
    def body(partial_time, brain_mask, rank_limit, start_basis):
        transform = spectral_table(partial_time.shape[-1] // 2)
        flags = brain_mask > 0
        pieces = coil_sum(partial_time, n_coil, n_slab)
        owns = jnp.stack([own.astype(jnp.bfloat16) for own, hop in pieces])
        hops = jnp.stack([hop for own, hop in pieces])
        spectra = jnp.einsum("bvt,tf->bvf", owns, transform, preferred_element_type=jnp.float32)
        spectra = spectra + jnp.einsum("bvt,tf->bvf", hops, transform, preferred_element_type=jnp.float32)
        return denoise_batch(spectra, flags, rank_limit, start_basis)

    return body


def solution(mesh):
    return jax.shard_map(
        make_body(mesh.shape["coil"], mesh.shape["slab"]),
        mesh=mesh,
        in_specs=(
            P("coil", None, "slab", None, None),
            P(("coil", "slab")),
            P(("coil", "slab")),
            P(),
        ),
        out_specs=P(("coil", "slab"), None, None),
        check_vma=False,
    )
```

```python
import math

import jax
import jax.numpy as jnp
from jax import lax
from jax.experimental import pallas as pl
from jax.experimental.pallas import tpu as pltpu
from jax.sharding import PartitionSpec as P

ITERS = 4
HI = lax.Precision.HIGH


def spectral_table(length):
    points = jnp.arange(length, dtype=jnp.int32)
    phase_index = points[:, None] * points[None, :] % length
    angles = phase_index.astype(jnp.float32) * (2.0 * math.pi / length)
    cosine = jnp.cos(angles) / math.sqrt(length)
    sine_part = jnp.sin(angles) / math.sqrt(length)
    upper_rows = jnp.concatenate([cosine, -sine_part], axis=1)
    lower_rows = jnp.concatenate([sine_part, cosine], axis=1)
    return jnp.concatenate([upper_rows, lower_rows], axis=0).astype(jnp.bfloat16)


def factor_solve_kernel(gram_ref, rhs_ref, out_ref):
    items = range(gram_ref.shape[0])
    grams = [gram_ref[item] for item in items]
    works = [rhs_ref[item] for item in items]
    for col in range(grams[0].shape[0]):
        for item in items:
            gram, work = grams[item], works[item]
            scale = 1.0 / jnp.sqrt(gram[col:col + 1, col:col + 1])
            column = gram[:, col:col + 1] * scale
            row = gram[col:col + 1, :] * scale
            solved = work[col:col + 1, :] * scale
            out_ref[item, col:col + 1, :] = solved
            grams[item] = gram - column * row
            works[item] = work - column * solved


def factor_solve(inner_gram, rhs):
    sym = 0.5 * (inner_gram + jnp.swapaxes(inner_gram, -1, -2))
    return pl.pallas_call(
        factor_solve_kernel,
        out_shape=jax.ShapeDtypeStruct(rhs.shape, jnp.float32),
        compiler_params=pltpu.CompilerParams(),
    )(sym, rhs)


def denoise_batch(spectra, flags, ranks, start_basis):
    kernel = jnp.einsum("bvf,bwf->bvw", spectra, spectra, precision=HI)
    coeff = jnp.einsum("kf,bvf->bkv", start_basis, spectra, precision=HI)
    for sweep_index in range(ITERS):
        pushed = jnp.einsum("bkv,bvw->bkw", coeff, kernel, precision=HI)
        inner_gram = jnp.einsum("bkw,bjw->bkj", pushed, coeff, precision=HI)
        if sweep_index < ITERS - 1:
            coeff = factor_solve(inner_gram, pushed)
        else:
            image = jnp.einsum("bkv,bvf->bkf", coeff, spectra, preferred_element_type=jnp.float32)
            both = factor_solve(inner_gram, jnp.concatenate([pushed, image], axis=-1))
            coeff = both[..., : pushed.shape[-1]]
            subspace = both[..., pushed.shape[-1]:]
    keep_rows = jnp.arange(subspace.shape[1], dtype=jnp.int32)[None, :, None] < ranks[:, None, None]
    truncated = jnp.where(keep_rows, subspace, 0.0)
    coefficients = jnp.where(keep_rows, coeff, 0.0)
    result = jnp.einsum("bkv,bkf->bvf", coefficients, truncated, preferred_element_type=jnp.float32)
    result = result.astype(jnp.bfloat16)
    return jnp.where(flags[:, None, None], result, jnp.zeros_like(result))


def ring_pairs(n_coil, n_slab):
    pairs = []
    for coil in range(n_coil):
        x_hi, core = divmod(coil, 2)
        for slab in range(n_slab):
            x_lo = slab % 2
            x = 2 * x_hi + x_lo
            step = 1 if core == 0 else -1
            x_to = (x + step) % 4
            coil_to = 2 * (x_to // 2) + core
            slab_to = slab - x_lo + x_to % 2
            pairs.append((coil * n_slab + slab, coil_to * n_slab + slab_to))
    return pairs


def coil_sum(partial_time, n_coil, n_slab):
    coil = lax.axis_index("coil")
    chip_pair = [(i, i ^ 1) for i in range(n_coil)]
    pairs = ring_pairs(n_coil, n_slab)
    patch_count = partial_time.shape[2]

    def pick(source, o, q):
        block = lax.dynamic_slice(source, (0, o, q, 0, 0), (1, 1, 1) + source.shape[3:])
        return block.reshape(source.shape[3:])

    forwards = []
    for q in range(patch_count):
        got_forward = lax.ppermute(pick(partial_time, coil ^ 3, q), "coil", chip_pair)
        forward = pick(partial_time, coil ^ 2, q).astype(jnp.float32) + got_forward.astype(jnp.float32)
        forwards.append(forward.astype(jnp.bfloat16))
    source, forwards = lax.optimization_barrier((partial_time, forwards))
    sums = []
    for q in range(patch_count):
        hop = lax.ppermute(forwards[q], ("coil", "slab"), pairs)
        hop = lax.ppermute(hop, ("coil", "slab"), pairs)
        got_own = lax.ppermute(pick(source, coil ^ 1, q), "coil", chip_pair)
        own = pick(source, coil, q).astype(jnp.float32) + got_own.astype(jnp.float32)
        sums.append((own, hop))
    return sums


def make_body(n_coil, n_slab):
    def body(partial_time, brain_mask, rank_limit, start_basis):
        transform = spectral_table(partial_time.shape[-1] // 2)
        flags = brain_mask > 0
        pieces = coil_sum(partial_time, n_coil, n_slab)
        owns = jnp.stack([own.astype(jnp.bfloat16) for own, hop in pieces])
        hops = jnp.stack([hop for own, hop in pieces])
        spectra = jnp.einsum("bvt,tf->bvf", owns, transform, preferred_element_type=jnp.float32)
        spectra = spectra + jnp.einsum("bvt,tf->bvf", hops, transform, preferred_element_type=jnp.float32)
        return denoise_batch(spectra, flags, rank_limit, start_basis)

    return body


def solution(mesh):
    return jax.shard_map(
        make_body(mesh.shape["coil"], mesh.shape["slab"]),
        mesh=mesh,
        in_specs=(
            P("coil", None, "slab", None, None),
            P(("coil", "slab")),
            P(("coil", "slab")),
            P(),
        ),
        out_specs=P(("coil", "slab"), None, None),
        check_vma=False,
    )
```

```python
import math

import jax
import jax.numpy as jnp
from jax import lax
from jax.experimental import pallas as pl
from jax.sharding import PartitionSpec as P

ITERS = 4
HI = lax.Precision.HIGH


def spectral_table(length):
    points = jnp.arange(length, dtype=jnp.int32)
    phase_index = points[:, None] * points[None, :] % length
    angles = phase_index.astype(jnp.float32) * (2.0 * math.pi / length)
    cosine = jnp.cos(angles) / math.sqrt(length)
    sine_part = jnp.sin(angles) / math.sqrt(length)
    upper_rows = jnp.concatenate([cosine, -sine_part], axis=1)
    lower_rows = jnp.concatenate([sine_part, cosine], axis=1)
    return jnp.concatenate([upper_rows, lower_rows], axis=0).astype(jnp.bfloat16)


def factor_solve_kernel(gram_ref, rhs_ref, out_ref):
    items = range(gram_ref.shape[0])
    grams = [gram_ref[item] for item in items]
    works = [rhs_ref[item] for item in items]
    for col in range(grams[0].shape[0]):
        for item in items:
            gram, work = grams[item], works[item]
            scale = 1.0 / jnp.sqrt(gram[col:col + 1, col:col + 1])
            column = gram[:, col:col + 1] * scale
            row = gram[col:col + 1, :] * scale
            solved = work[col:col + 1, :] * scale
            out_ref[item, col:col + 1, :] = solved
            grams[item] = gram - column * row
            works[item] = work - column * solved


def factor_solve(inner_gram, rhs):
    sym = 0.5 * (inner_gram + jnp.swapaxes(inner_gram, -1, -2))
    return pl.pallas_call(
        factor_solve_kernel,
        out_shape=jax.ShapeDtypeStruct(rhs.shape, jnp.float32),
    )(sym, rhs)


def denoise_batch(spectra, flags, ranks, start_basis):
    kernel = jnp.einsum("bvf,bwf->bvw", spectra, spectra, precision=HI)
    coeff = jnp.einsum("kf,bvf->bkv", start_basis, spectra, precision=HI)
    for sweep_index in range(ITERS):
        pushed = jnp.einsum("bkv,bvw->bkw", coeff, kernel, precision=HI)
        inner_gram = jnp.einsum("bkw,bjw->bkj", pushed, coeff, precision=HI)
        if sweep_index < ITERS - 1:
            coeff = factor_solve(inner_gram, pushed)
        else:
            image = jnp.einsum("bkv,bvf->bkf", coeff, spectra, preferred_element_type=jnp.float32)
            both = factor_solve(inner_gram, jnp.concatenate([pushed, image], axis=-1))
            coeff = both[..., : pushed.shape[-1]]
            subspace = both[..., pushed.shape[-1]:]
    keep_rows = jnp.arange(subspace.shape[1], dtype=jnp.int32)[None, :, None] < ranks[:, None, None]
    truncated = jnp.where(keep_rows, subspace, 0.0)
    coefficients = jnp.where(keep_rows, coeff, 0.0)
    result = jnp.einsum("bkv,bkf->bvf", coefficients, truncated, preferred_element_type=jnp.float32)
    result = result.astype(jnp.bfloat16)
    return jnp.where(flags[:, None, None], result, jnp.zeros_like(result))


def ring_pairs(n_coil, n_slab):
    pairs = []
    for coil in range(n_coil):
        x_hi, core = divmod(coil, 2)
        for slab in range(n_slab):
            x_lo = slab % 2
            x = 2 * x_hi + x_lo
            step = 1 if core == 0 else -1
            x_to = (x + step) % 4
            coil_to = 2 * (x_to // 2) + core
            slab_to = slab - x_lo + x_to % 2
            pairs.append((coil * n_slab + slab, coil_to * n_slab + slab_to))
    return pairs


def coil_sum(partial_time, n_coil, n_slab):
    coil = lax.axis_index("coil")
    chip_pair = [(i, i ^ 1) for i in range(n_coil)]
    pairs = ring_pairs(n_coil, n_slab)
    patch_count = partial_time.shape[2]

    def pick(source, o, q):
        block = lax.dynamic_slice(source, (0, o, q, 0, 0), (1, 1, 1) + source.shape[3:])
        return block.reshape(source.shape[3:])

    forwards = []
    for q in range(patch_count):
        got_forward = lax.ppermute(pick(partial_time, coil ^ 3, q), "coil", chip_pair)
        forward = pick(partial_time, coil ^ 2, q).astype(jnp.float32) + got_forward.astype(jnp.float32)
        forwards.append(forward.astype(jnp.bfloat16))
    source, forwards = lax.optimization_barrier((partial_time, forwards))
    sums = []
    for q in range(patch_count):
        hop = lax.ppermute(forwards[q], ("coil", "slab"), pairs)
        hop = lax.ppermute(hop, ("coil", "slab"), pairs)
        got_own = lax.ppermute(pick(source, coil ^ 1, q), "coil", chip_pair)
        own = pick(source, coil, q).astype(jnp.float32) + got_own.astype(jnp.float32)
        sums.append((own, hop))
    return sums


def make_body(n_coil, n_slab):
    def body(partial_time, brain_mask, rank_limit, start_basis):
        transform = spectral_table(partial_time.shape[-1] // 2)
        flags = brain_mask > 0
        pieces = coil_sum(partial_time, n_coil, n_slab)
        owns = jnp.stack([own.astype(jnp.bfloat16) for own, hop in pieces])
        spectra = jnp.einsum("bvt,tf->bvf", owns, transform, preferred_element_type=jnp.float32)
        spectra = jnp.stack([
            spectra[q] + jnp.dot(hop, transform, preferred_element_type=jnp.float32)
            for q, (own, hop) in enumerate(pieces)
        ])
        return denoise_batch(spectra, flags, rank_limit, start_basis)

    return body


def solution(mesh):
    return jax.shard_map(
        make_body(mesh.shape["coil"], mesh.shape["slab"]),
        mesh=mesh,
        in_specs=(
            P("coil", None, "slab", None, None),
            P(("coil", "slab")),
            P(("coil", "slab")),
            P(),
        ),
        out_specs=P(("coil", "slab"), None, None),
        check_vma=False,
    )
```
